512 devices in a mesh: row: 64 (over z, y), col: 8 (over x, core).
Axes of the slice: x: 4, y: 8, z: 8, core: 2. Of those that a mesh axis runs over, the one named last changes fastest.
Arguments:
- tiles: float32 [64, 8, 64, 128, 128], P('row', 'col'), may hold values from -0.0625 to 0.0625
- tile_rows: int32 [64, 8, 64], P('row', 'col'), may hold values from 0 to 15, as said below
- tile_cols: int32 [64, 8, 64], P('row', 'col'), may hold values from 0 to 63, as said below
- exponents: int32 [65536], P('col'), may hold values from 0 to 3
- u_basis: float32 [64, 131072], P(None, 'row'), may hold values from -6 to 6
- v_basis: float32 [64, 65536], P(None, ('col', 'row')), may hold values from -6 to 6
- prior: float32 [64, 64], replicated, may hold values from -0.75 to 0.75
Outputs:
- u_next: float32 [64, 131072], P(None, ('row', 'col'))
- v_next: float32 [64, 65536], P(None, ('col', 'row'))
- v_factor: float32 [64, 64], replicated
- u_factor: float32 [64, 64], replicated
The draws below stay inside these ranges and needn't reach their ends.
Inputs may be any that keep to these rules, and one draw needn't show every extreme that they name: `tile_rows`: within each grid cell every tile row of 0 to 15 appears exactly 64 / 16 times. `tile_cols`: within each grid cell every tile column of 0 to 63 appears exactly 64 / 64 times.
All inputs are finite; a program needn't handle non-finite values.
Results may differ from the reference program's by a relative error of at most 0.00018.
Values sent between devices are 32-bit elements; how exact they have to be, the bound alone decides.
No kernel may reach another device: no remote copies, remote signals or barrier semaphores. Data moves between devices by JAX's collectives and lax.ppermute only.
A program may use at most 64 MiB of HBM per device.

```python
import math
import jax
import jax.numpy as jnp
from jax import lax

S = 64
TILE = 128
RT = 16
CT = 64
NT = 64
GR = 64
GC = 8
M = 131072
N = 65536
N_ROW = 64


def covering(key, length):
    repeats = NT // length
    keys = jax.random.split(key, GR * GC * repeats)
    perms = jax.vmap(lambda k: jax.random.permutation(k, length))(keys)
    return perms.reshape(GR, GC, NT).astype(jnp.int32)


def draw_tile_rows(key, part):
    return covering(jax.random.fold_in(key, 11), RT)


def draw_tile_cols(key, part):
    return covering(jax.random.fold_in(key, 23), CT)


def place_ends(result, own_key, least, largest):
    dims = result.shape
    index_at = [jax.random.randint(jax.random.fold_in(own_key, axis), (), 0, dims[axis]) for axis in range(len(dims))]
    result = result.at[tuple(index_at)].set(least)
    longest = dims.index(max(dims))
    index_at[longest] = (index_at[longest] + 1) % dims[longest]
    return result.at[tuple(index_at)].set(largest)


def level_of(key, extent, cuts, low, top_value):
    def one(position, shards_of):
        heights = jax.random.uniform(jax.random.fold_in(jax.random.fold_in(key, 6), position), (shards_of,), jnp.float32, low / len(cuts), top_value / len(cuts))
        return jnp.repeat(jnp.exp(heights), extent[position] // shards_of).reshape((-1,) + (1,) * (len(extent) - position - 1))

    factor_of = one(*cuts[0])
    for cut in cuts[1:]:
        factor_of = factor_of * one(*cut)
    return factor_of


def gaussian(own_key, dims, deviation, most, cuts=(), dtype=jnp.bfloat16):
    loudness = level_of(own_key, dims, cuts, -0.22, 0.18) if cuts else 1.0
    drawn = jax.random.normal(own_key, dims, jnp.float32) * deviation * loudness
    return jnp.minimum(jnp.maximum(drawn, -most), most).astype(dtype)


def setup_inputs(seed: int = 0) -> dict:
    seeds = jax.random.split(jax.random.key(seed), 8)
    tiles = gaussian(seeds[0], (GR, GC, NT, TILE, TILE), (N_ROW * NT * TILE // CT) ** -0.5, 0.0625, ((0, 64), (1, 8)), jnp.float32)
    tile_rows = draw_tile_rows(jax.random.fold_in(seeds[7], 71), 0)
    tile_cols = draw_tile_cols(jax.random.fold_in(seeds[7], 71), 0)
    exponents = place_ends(jax.random.randint(seeds[3], (N,), 0, 4), jax.random.fold_in(seeds[3], 1), 0, 3).astype(jnp.int32)
    u_basis = gaussian(seeds[4], (S, M), 1.0, 6.0, ((1, 64),), jnp.float32)
    v_basis = gaussian(seeds[5], (S, N), 1.0, 6.0, ((1, 512),), jnp.float32)
    prior = gaussian(seeds[6], (S, S), S ** -0.5, 0.75, (), jnp.float32)
    return dict(tiles=tiles, tile_rows=tile_rows, tile_cols=tile_cols, exponents=exponents, u_basis=u_basis, v_basis=v_basis, prior=prior)


HIGH = lax.Precision.HIGHEST

def lower_solve(factor, rhs):
    return lax.linalg.triangular_solve(factor, rhs, left_side=True, lower=True)

def reference(tiles, tile_rows, tile_cols, exponents, u_basis, v_basis, prior):
    grid_rows, grid_cols, count, tl, _ = tiles.shape
    width, total_rows = u_basis.shape
    total_cols = v_basis.shape[1]
    tile_cols_all = total_cols // tl
    rows_tiles = total_rows // (grid_rows * tl)
    cols_tiles = tile_cols_all // grid_cols
    col_scale = jnp.exp2(-exponents.astype(jnp.float32))
    lowtri = jnp.tril(prior)
    offsets = (jnp.arange(grid_cols) * cols_tiles).astype(jnp.int32)
    global_cols = (tile_cols + offsets[None, :, None]).astype(jnp.int32)
    u_blocks = u_basis.reshape(width, grid_rows, rows_tiles, tl).transpose(1, 0, 2, 3)

    def left_step(acc, inputs):
        tile_r, rows_r, gcol_r, ublock = inputs
        picked = jnp.take(ublock, rows_r.reshape(-1), axis=1)
        prod = jnp.einsum('sta,tab->tsb', picked, tile_r.reshape(-1, tl, tl), precision=HIGH)
        acc = acc + jax.ops.segment_sum(prod, gcol_r.reshape(-1), num_segments=tile_cols_all)
        return (acc, None)
    acc0 = jnp.zeros((tile_cols_all, width, tl), jnp.float32)
    acc, _ = lax.scan(left_step, acc0, (tiles, tile_rows, global_cols, u_blocks))
    left = acc.transpose(1, 0, 2).reshape(width, total_cols) * col_scale
    pt = left - jnp.dot(lowtri, v_basis, precision=HIGH)
    gram = jnp.dot(pt, pt.T, precision=HIGH)
    v_factor = jnp.linalg.cholesky(gram / total_cols)
    v_next = lower_solve(v_factor, pt)
    scaled = (v_next * col_scale).reshape(width, tile_cols_all, tl)

    def right_step(carry, inputs):
        tile_r, rows_r, gcol_r = inputs
        picked = jnp.take(scaled, gcol_r.reshape(-1), axis=1)
        prod = jnp.einsum('stb,tab->tsa', picked, tile_r.reshape(-1, tl, tl), precision=HIGH)
        return (carry, jax.ops.segment_sum(prod, rows_r.reshape(-1), num_segments=rows_tiles))
    _, pieces = lax.scan(right_step, jnp.zeros((), jnp.float32), (tiles, tile_rows, global_cols))
    right = pieces.transpose(2, 0, 1, 3).reshape(width, total_rows)
    factor = math.sqrt(total_rows / total_cols)
    qt = factor * right - jnp.dot(v_factor.T, u_basis, precision=HIGH)
    ugram = jnp.dot(qt, qt.T, precision=HIGH)
    u_factor = jnp.linalg.cholesky(ugram / total_rows)
    u_next = lower_solve(u_factor, qt)
    return (u_next, v_next, v_factor, u_factor)
```

```python
import math

import jax
import jax.numpy as jnp
from jax import lax
from jax.sharding import PartitionSpec as P

HIGH = lax.Precision.HIGHEST


def lower_solve(factor, rhs):
    return lax.linalg.triangular_solve(factor, rhs, left_side=True, lower=True)


def butterfly_sum(x, axis):
    n = lax.axis_size(axis)
    k = 1
    while k < n:
        x = x + lax.ppermute(x, axis, [(i, i ^ k) for i in range(n)])
        k *= 2
    return x


def per_device(tiles, tile_rows, tile_cols, exponents, u_basis, v_basis, prior):
    local_tiles = tiles[0, 0]
    rows_here = tile_rows[0, 0]
    cols_here = tile_cols[0, 0]
    count, tl, _ = local_tiles.shape
    width, block_rows = u_basis.shape
    block_cols = exponents.shape[0]
    rows_tiles = block_rows // tl
    cols_tiles = block_cols // tl
    n_row = lax.axis_size("row")
    n_col = lax.axis_size("col")
    total_rows = block_rows * n_row
    total_cols = block_cols * n_col
    v_piece = v_basis.shape[1]
    u_piece = block_rows // n_col
    col_scale = jnp.exp2(-exponents.astype(jnp.float32))
    lowtri = jnp.tril(prior)
    col_hits = (cols_here[:, None] == jnp.arange(cols_tiles, dtype=jnp.int32)[None, :]).astype(
        jnp.float32
    )
    row_hits = (rows_here[:, None] == jnp.arange(rows_tiles, dtype=jnp.int32)[None, :]).astype(
        jnp.float32
    )
    picked = jnp.take(u_basis.reshape(width, rows_tiles, tl), rows_here, axis=1)
    prod = jnp.einsum("sta,tab->stb", picked, local_tiles, precision=HIGH)
    partial = jnp.einsum("stb,tc->csb", prod, col_hits, precision=HIGH).reshape(
        n_row, v_piece // tl, width, tl
    )
    partial = (partial * col_scale.reshape(n_row, v_piece // tl, 1, tl)).transpose(0, 2, 1, 3)
    partial = partial.reshape(n_row, width, v_piece)
    received = lax.all_to_all(partial, "row", 0, 0, tiled=True)
    pt_piece = received.sum(0) - jnp.dot(lowtri, v_basis, precision=HIGH)
    spread = jnp.broadcast_to(pt_piece[None], (n_row, width, v_piece))
    column = lax.all_to_all(spread, "row", 0, 0, tiled=True)
    gram = butterfly_sum(jnp.einsum("jsb,jtb->st", column, column, precision=HIGH), "col")
    v_factor = jnp.linalg.cholesky(gram / total_cols)
    pt_column = column.transpose(1, 0, 2).reshape(width, block_cols)
    v_column = lower_solve(v_factor, pt_column)
    offset = lax.axis_index("row") * v_piece
    v_next = lax.dynamic_slice_in_dim(v_column, offset, v_piece, 1)
    factor = math.sqrt(total_rows / total_cols)
    scaled = (v_column * col_scale).reshape(width, cols_tiles, tl)
    chosen = jnp.take(scaled, cols_here, axis=1)
    products = jnp.einsum("stb,tab->sta", chosen, local_tiles, precision=HIGH)
    terms = factor * jnp.einsum("sta,tr->rsa", products, row_hits, precision=HIGH)
    terms = terms.reshape(n_col, u_piece // tl, width, tl).transpose(0, 2, 1, 3)
    terms = terms.reshape(n_col, width, u_piece)
    summed = lax.all_to_all(terms, "col", 0, 0, tiled=True).sum(0)
    u_own = lax.dynamic_slice_in_dim(u_basis, lax.axis_index("col") * u_piece, u_piece, 1)
    qt_piece = summed - jnp.dot(v_factor.T, u_own, precision=HIGH)
    ugram = jnp.dot(qt_piece, qt_piece.T, precision=HIGH)
    ugram = butterfly_sum(butterfly_sum(ugram, "col"), "row")
    u_factor = jnp.linalg.cholesky(ugram / total_rows)
    u_next = lower_solve(u_factor, qt_piece)
    return (u_next, v_next, v_factor, u_factor)


def solution(mesh):
    placed = (
        P("row", "col", None, None, None),
        P("row", "col", None),
        P("row", "col", None),
        P("col"),
        P(None, "row"),
        P(None, ("col", "row")),
        P(),
    )
    return jax.shard_map(
        per_device,
        mesh=mesh,
        in_specs=placed,
        out_specs=(P(None, ("row", "col")), P(None, ("col", "row")), P(), P()),
        check_vma=False,
    )
```

```python
import math

import jax
import jax.numpy as jnp
from jax import lax
from jax.sharding import PartitionSpec as P

HIGH = lax.Precision.HIGHEST


def lower_solve(factor, rhs):
    return lax.linalg.triangular_solve(factor, rhs, left_side=True, lower=True)


ROW = ("row_hi", "row_lo")


def gather_sum(x, axis):
    n = lax.axis_size(axis)
    return lax.all_to_all(jnp.broadcast_to(x[None], (n,) + x.shape), axis, 0, 0, tiled=True).sum(0)


def per_device(tiles, tile_rows, tile_cols, exponents, u_basis, v_basis, prior):
    local_tiles = tiles[0, 0]
    rows_here = tile_rows[0, 0]
    cols_here = tile_cols[0, 0]
    count, tl, _ = local_tiles.shape
    width, block_rows = u_basis.shape
    block_cols = exponents.shape[0]
    rows_tiles = block_rows // tl
    cols_tiles = block_cols // tl
    n_row = lax.axis_size(ROW)
    n_col = lax.axis_size("col")
    total_rows = block_rows * n_row
    total_cols = block_cols * n_col
    v_piece = v_basis.shape[1]
    u_piece = block_rows // n_col
    col_scale = jnp.exp2(-exponents.astype(jnp.float32))
    lowtri = jnp.tril(prior)
    col_hits = (cols_here[:, None] == jnp.arange(cols_tiles, dtype=jnp.int32)[None, :]).astype(
        jnp.float32
    )
    row_hits = (rows_here[:, None] == jnp.arange(rows_tiles, dtype=jnp.int32)[None, :]).astype(
        jnp.float32
    )
    picked = jnp.take(u_basis.reshape(width, rows_tiles, tl), rows_here, axis=1)
    prod = jnp.einsum("sta,tab->stb", picked, local_tiles, precision=HIGH)
    partial = jnp.einsum("stb,tc->csb", prod, col_hits, precision=HIGH).reshape(
        n_row, v_piece // tl, width, tl
    )
    partial = (partial * col_scale.reshape(n_row, v_piece // tl, 1, tl)).transpose(0, 2, 1, 3)
    partial = partial.reshape(n_row, width, v_piece)
    received = lax.all_to_all(partial, ROW, 0, 0, tiled=True)
    pt_piece = received.sum(0) - jnp.dot(lowtri, v_basis, precision=HIGH)
    spread = jnp.broadcast_to(pt_piece[None], (n_row, width, v_piece))
    column = lax.all_to_all(spread, ROW, 0, 0, tiled=True)
    gram = gather_sum(jnp.einsum("jsb,jtb->st", column, column, precision=HIGH), "col")
    v_factor = jnp.linalg.cholesky(gram / total_cols)
    pt_column = column.transpose(1, 0, 2).reshape(width, block_cols)
    v_column = lower_solve(v_factor, pt_column)
    offset = lax.axis_index(ROW) * v_piece
    v_next = lax.dynamic_slice_in_dim(v_column, offset, v_piece, 1)
    factor = math.sqrt(total_rows / total_cols)
    scaled = (v_column * col_scale).reshape(width, cols_tiles, tl)
    chosen = jnp.take(scaled, cols_here, axis=1)
    products = jnp.einsum("stb,tab->sta", chosen, local_tiles, precision=HIGH)
    terms = factor * jnp.einsum("sta,tr->rsa", products, row_hits, precision=HIGH)
    terms = terms.reshape(n_col, u_piece // tl, width, tl).transpose(0, 2, 1, 3)
    terms = terms.reshape(n_col, width, u_piece)
    summed = lax.all_to_all(terms, "col", 0, 0, tiled=True).sum(0)
    u_own = lax.dynamic_slice_in_dim(u_basis, lax.axis_index("col") * u_piece, u_piece, 1)
    qt_piece = summed - jnp.dot(v_factor.T, u_own, precision=HIGH)
    ugram = jnp.dot(qt_piece, qt_piece.T, precision=HIGH)
    ugram = gather_sum(gather_sum(gather_sum(ugram, "col"), "row_lo"), "row_hi")
    u_factor = jnp.linalg.cholesky(ugram / total_rows)
    u_next = lower_solve(u_factor, qt_piece)
    return (u_next, v_next, v_factor, u_factor)


def solution(mesh):
    n_row = mesh.shape["row"]
    n_col = mesh.shape["col"]
    lo = 1
    while lo * lo < n_row:
        lo *= 2
    grid = jax.sharding.Mesh(mesh.devices.reshape(n_row // lo, lo, n_col), ROW + ("col",))
    placed = (
        P(ROW, "col", None, None, None),
        P(ROW, "col", None),
        P(ROW, "col", None),
        P("col"),
        P(None, ROW),
        P(None, ("col",) + ROW),
        P(),
    )
    return jax.shard_map(
        per_device,
        mesh=grid,
        in_specs=placed,
        out_specs=(P(None, ROW + ("col",)), P(None, ("col",) + ROW), P(), P()),
        check_vma=False,
    )
```

```python
import math

import jax
import jax.numpy as jnp
from jax import lax
from jax.sharding import PartitionSpec as P

HIGH = lax.Precision.HIGHEST
FAST = lax.Precision.HIGH


def lower_solve(factor, rhs):
    return lax.linalg.triangular_solve(factor, rhs, left_side=True, lower=True)


ROW = ("row_hi", "row_lo")


def gather_sum(x, axis):
    n = lax.axis_size(axis)
    return lax.all_to_all(jnp.broadcast_to(x[None], (n,) + x.shape), axis, 0, 0, tiled=True).sum(0)


def per_device(tiles, tile_rows, tile_cols, exponents, u_basis, v_basis, prior):
    local_tiles = tiles[0, 0]
    rows_here = tile_rows[0, 0]
    cols_here = tile_cols[0, 0]
    count, tl, _ = local_tiles.shape
    width, block_rows = u_basis.shape
    block_cols = exponents.shape[0]
    rows_tiles = block_rows // tl
    cols_tiles = block_cols // tl
    n_row = lax.axis_size(ROW)
    n_col = lax.axis_size("col")
    total_rows = block_rows * n_row
    total_cols = block_cols * n_col
    v_piece = v_basis.shape[1]
    u_piece = block_rows // n_col
    col_scale = jnp.exp2(-exponents.astype(jnp.float32))
    lowtri = jnp.tril(prior)
    col_hits = (cols_here[:, None] == jnp.arange(cols_tiles, dtype=jnp.int32)[None, :]).astype(
        jnp.float32
    )
    row_hits = (rows_here[:, None] == jnp.arange(rows_tiles, dtype=jnp.int32)[None, :]).astype(
        jnp.float32
    )
    picked = jnp.take(u_basis.reshape(width, rows_tiles, tl), rows_here, axis=1)
    prod = jnp.einsum("sta,tab->stb", picked, local_tiles, precision=FAST)
    partial = jnp.einsum("stb,tc->csb", prod, col_hits, precision=FAST).reshape(
        n_row, v_piece // tl, width, tl
    )
    partial = (partial * col_scale.reshape(n_row, v_piece // tl, 1, tl)).transpose(0, 2, 1, 3)
    partial = partial.reshape(n_row, width, v_piece)
    received = lax.all_to_all(partial, ROW, 0, 0, tiled=True)
    pt_piece = received.sum(0) - jnp.dot(lowtri, v_basis, precision=HIGH)
    spread = jnp.broadcast_to(pt_piece[None], (n_row, width, v_piece))
    column = lax.all_to_all(spread, ROW, 0, 0, tiled=True)
    gram = gather_sum(jnp.einsum("jsb,jtb->st", column, column, precision=HIGH), "col")
    v_factor = jnp.linalg.cholesky(gram / total_cols)
    pt_column = column.transpose(1, 0, 2).reshape(width, block_cols)
    v_column = lower_solve(v_factor, pt_column)
    offset = lax.axis_index(ROW) * v_piece
    v_next = lax.dynamic_slice_in_dim(v_column, offset, v_piece, 1)
    factor = math.sqrt(total_rows / total_cols)
    scaled = (v_column * col_scale).reshape(width, cols_tiles, tl)
    chosen = jnp.take(scaled, cols_here, axis=1)
    products = jnp.einsum("stb,tab->sta", chosen, local_tiles, precision=FAST)
    terms = factor * jnp.einsum("sta,tr->rsa", products, row_hits, precision=FAST)
    terms = terms.reshape(n_col, u_piece // tl, width, tl).transpose(0, 2, 1, 3)
    terms = terms.reshape(n_col, width, u_piece)
    summed = lax.all_to_all(terms, "col", 0, 0, tiled=True).sum(0)
    u_own = lax.dynamic_slice_in_dim(u_basis, lax.axis_index("col") * u_piece, u_piece, 1)
    qt_piece = summed - jnp.dot(v_factor.T, u_own, precision=HIGH)
    ugram = jnp.dot(qt_piece, qt_piece.T, precision=HIGH)
    ugram = gather_sum(gather_sum(gather_sum(ugram, "col"), "row_lo"), "row_hi")
    u_factor = jnp.linalg.cholesky(ugram / total_rows)
    u_next = lower_solve(u_factor, qt_piece)
    return (u_next, v_next, v_factor, u_factor)


def solution(mesh):
    n_row = mesh.shape["row"]
    n_col = mesh.shape["col"]
    lo = 1
    while lo * lo < n_row:
        lo *= 2
    grid = jax.sharding.Mesh(mesh.devices.reshape(n_row // lo, lo, n_col), ROW + ("col",))
    placed = (
        P(ROW, "col", None, None, None),
        P(ROW, "col", None),
        P(ROW, "col", None),
        P("col"),
        P(None, ROW),
        P(None, ("col",) + ROW),
        P(),
    )
    return jax.shard_map(
        per_device,
        mesh=grid,
        in_specs=placed,
        out_specs=(P(None, ROW + ("col",)), P(None, ("col",) + ROW), P(), P()),
        check_vma=False,
    )
```

```python
import math

import jax
import jax.numpy as jnp
from jax import lax
from jax.sharding import PartitionSpec as P

HIGH = lax.Precision.HIGHEST
FAST = lax.Precision.HIGH


def lower_solve(factor, rhs):
    return lax.linalg.triangular_solve(factor, rhs, left_side=True, lower=True)


ROW = ("row_hi", "row_lo")


def gather_sum(x, axis):
    n = lax.axis_size(axis)
    return lax.all_to_all(jnp.broadcast_to(x[None], (n,) + x.shape), axis, 0, 0, tiled=True).sum(0)


def per_device(tiles, tile_rows, tile_cols, exponents, u_basis, v_basis, prior):
    local_tiles = tiles[0, 0]
    rows_here = tile_rows[0, 0]
    cols_here = tile_cols[0, 0]
    count, tl, _ = local_tiles.shape
    width, block_rows = u_basis.shape
    block_cols = exponents.shape[0]
    rows_tiles = block_rows // tl
    cols_tiles = block_cols // tl
    n_row = lax.axis_size(ROW)
    n_col = lax.axis_size("col")
    total_rows = block_rows * n_row
    total_cols = block_cols * n_col
    v_piece = v_basis.shape[1]
    u_piece = block_rows // n_col
    col_scale = jnp.exp2(-exponents.astype(jnp.float32))
    lowtri = jnp.tril(prior)
    col_hits = (cols_here[:, None] == jnp.arange(cols_tiles, dtype=jnp.int32)[None, :]).astype(
        jnp.float32
    )
    row_hits = (rows_here[:, None] == jnp.arange(rows_tiles, dtype=jnp.int32)[None, :]).astype(
        jnp.float32
    )
    picked = jnp.take(u_basis.reshape(width, rows_tiles, tl), rows_here, axis=1)
    prod = jnp.einsum("sta,tab->stb", picked, local_tiles, precision=FAST)
    partial = jnp.einsum("stb,tc->csb", prod, col_hits, precision=FAST).reshape(
        n_row, v_piece // tl, width, tl
    )
    partial = (partial * col_scale.reshape(n_row, v_piece // tl, 1, tl)).transpose(0, 2, 1, 3)
    partial = partial.reshape(n_row, width, v_piece)
    received = lax.all_to_all(partial, ROW, 0, 0, tiled=True)
    pt_piece = received.sum(0) - jnp.dot(lowtri, v_basis, precision=HIGH)
    spread = jnp.broadcast_to(pt_piece[None], (n_row, width, v_piece))
    column = lax.all_to_all(spread, ROW, 0, 0, tiled=True)
    gram = gather_sum(jnp.einsum("jsb,jtb->st", column, column, precision=HIGH), "col")
    v_factor = jnp.linalg.cholesky(gram / total_cols)
    v_next = lower_solve(v_factor, pt_piece)
    factor = math.sqrt(total_rows / total_cols)
    scaled = column.transpose(1, 0, 2).reshape(width, block_cols) * col_scale
    chosen = jnp.take(scaled.reshape(width, cols_tiles, tl), cols_here, axis=1)
    products = jnp.einsum("stb,tab->sta", chosen, local_tiles, precision=FAST)
    terms = jnp.einsum("sta,tr->rsa", products, row_hits, precision=FAST)
    terms = terms.reshape(n_col, u_piece // tl, width, tl).transpose(0, 2, 1, 3)
    terms = terms.reshape(n_col, width, u_piece)
    summed = lax.all_to_all(terms, "col", 0, 0, tiled=True).sum(0)
    u_own = lax.dynamic_slice_in_dim(u_basis, lax.axis_index("col") * u_piece, u_piece, 1)
    qt_piece = factor * lower_solve(v_factor, summed) - jnp.dot(v_factor.T, u_own, precision=HIGH)
    ugram = jnp.dot(qt_piece, qt_piece.T, precision=HIGH)
    ugram = gather_sum(gather_sum(gather_sum(ugram, "col"), "row_lo"), "row_hi")
    u_factor = jnp.linalg.cholesky(ugram / total_rows)
    u_next = lower_solve(u_factor, qt_piece)
    return (u_next, v_next, v_factor, u_factor)


def solution(mesh):
    n_row = mesh.shape["row"]
    n_col = mesh.shape["col"]
    lo = 1
    while lo * lo < n_row:
        lo *= 2
    grid = jax.sharding.Mesh(mesh.devices.reshape(n_row // lo, lo, n_col), ROW + ("col",))
    placed = (
        P(ROW, "col", None, None, None),
        P(ROW, "col", None),
        P(ROW, "col", None),
        P("col"),
        P(None, ROW),
        P(None, ("col",) + ROW),
        P(),
    )
    return jax.shard_map(
        per_device,
        mesh=grid,
        in_specs=placed,
        out_specs=(P(None, ROW + ("col",)), P(None, ("col",) + ROW), P(), P()),
        check_vma=False,
    )
```

```python
import math

import jax
import jax.numpy as jnp
from jax import lax
from jax.experimental import pallas as pl
from jax.experimental.pallas import tpu as pltpu
from jax.sharding import PartitionSpec as P

HIGH = lax.Precision.HIGHEST
FAST = lax.Precision.HIGH


def _factor_kernel(aug_ref, low_ref, inv_ref, work_ref):
    n = aug_ref.shape[0]
    work_ref[...] = aug_ref[...]
    lane = lax.broadcasted_iota(jnp.int32, aug_ref.shape, 1)
    sub = lax.broadcasted_iota(jnp.int32, (n, 1), 0)
    lane_row = lax.broadcasted_iota(jnp.int32, (1, aug_ref.shape[1]), 1)

    def step(j, low):
        whole = work_ref[...]
        row = work_ref[pl.ds(j, 1), :]
        pivot = jnp.sum(jnp.where(lane_row == j, row, 0.0), axis=1, keepdims=True)
        scale = 1.0 / jnp.sqrt(pivot)
        scaled_row = row * scale
        inv_ref[pl.ds(j, 1), :] = scaled_row
        column = jnp.sum(jnp.where(lane == j, whole, 0.0), axis=1, keepdims=True) * scale
        work_ref[...] = whole - jnp.where(sub > j, column, 0.0) * scaled_row
        return jnp.where(lane == j, jnp.where(sub >= j, column, 0.0), low)

    low_ref[...] = lax.fori_loop(0, n, step, jnp.zeros(aug_ref.shape, jnp.float32))


def cholesky_and_inverse(gram):
    n = gram.shape[0]
    aug = jnp.concatenate([gram, jnp.eye(n, dtype=jnp.float32)], axis=1)
    low, inv = pl.pallas_call(
        _factor_kernel,
        out_shape=(
            jax.ShapeDtypeStruct(aug.shape, jnp.float32),
            jax.ShapeDtypeStruct(aug.shape, jnp.float32),
        ),
        scratch_shapes=[pltpu.VMEM(aug.shape, jnp.float32)],
    )(aug)
    return low[:, :n], inv[:, n:]


ROW = ("row_hi", "row_lo")


def gather_sum(x, axis):
    n = lax.axis_size(axis)
    return lax.all_to_all(jnp.broadcast_to(x[None], (n,) + x.shape), axis, 0, 0, tiled=True).sum(0)


def per_device(tiles, tile_rows, tile_cols, exponents, u_basis, v_basis, prior):
    local_tiles = tiles[0, 0]
    rows_here = tile_rows[0, 0]
    cols_here = tile_cols[0, 0]
    count, tl, _ = local_tiles.shape
    width, block_rows = u_basis.shape
    block_cols = exponents.shape[0]
    rows_tiles = block_rows // tl
    cols_tiles = block_cols // tl
    n_row = lax.axis_size(ROW)
    n_col = lax.axis_size("col")
    total_rows = block_rows * n_row
    total_cols = block_cols * n_col
    v_piece = v_basis.shape[1]
    u_piece = block_rows // n_col
    col_scale = jnp.exp2(-exponents.astype(jnp.float32))
    lowtri = jnp.tril(prior)
    col_hits = (cols_here[:, None] == jnp.arange(cols_tiles, dtype=jnp.int32)[None, :]).astype(
        jnp.float32
    )
    row_hits = (rows_here[:, None] == jnp.arange(rows_tiles, dtype=jnp.int32)[None, :]).astype(
        jnp.float32
    )
    picked = jnp.take(u_basis.reshape(width, rows_tiles, tl), rows_here, axis=1)
    prod = jnp.einsum("sta,tab->stb", picked, local_tiles, precision=FAST)
    partial = jnp.einsum("stb,tc->csb", prod, col_hits, precision=FAST).reshape(
        n_row, v_piece // tl, width, tl
    )
    partial = (partial * col_scale.reshape(n_row, v_piece // tl, 1, tl)).transpose(0, 2, 1, 3)
    partial = partial.reshape(n_row, width, v_piece)
    received = lax.all_to_all(partial, ROW, 0, 0, tiled=True)
    pt_piece = received.sum(0) - jnp.dot(lowtri, v_basis, precision=HIGH)
    spread = jnp.broadcast_to(pt_piece[None], (n_row, width, v_piece))
    column = lax.all_to_all(spread, ROW, 0, 0, tiled=True)
    gram = gather_sum(jnp.einsum("jsb,jtb->st", column, column, precision=HIGH), "col")
    v_factor, v_inverse = cholesky_and_inverse(gram / total_cols)
    v_next = jnp.dot(v_inverse, pt_piece, precision=HIGH)
    factor = math.sqrt(total_rows / total_cols)
    scaled = column.transpose(1, 0, 2).reshape(width, block_cols) * col_scale
    chosen = jnp.take(scaled.reshape(width, cols_tiles, tl), cols_here, axis=1)
    products = jnp.einsum("stb,tab->sta", chosen, local_tiles, precision=FAST)
    terms = jnp.einsum("sta,tr->rsa", products, row_hits, precision=FAST)
    terms = terms.reshape(n_col, u_piece // tl, width, tl).transpose(0, 2, 1, 3)
    terms = terms.reshape(n_col, width, u_piece)
    summed = lax.all_to_all(terms, "col", 0, 0, tiled=True).sum(0)
    u_own = lax.dynamic_slice_in_dim(u_basis, lax.axis_index("col") * u_piece, u_piece, 1)
    qt_piece = factor * jnp.dot(v_inverse, summed, precision=HIGH) - jnp.dot(v_factor.T, u_own, precision=HIGH)
    ugram = jnp.dot(qt_piece, qt_piece.T, precision=HIGH)
    ugram = gather_sum(gather_sum(gather_sum(ugram, "col"), "row_lo"), "row_hi")
    u_factor, u_inverse = cholesky_and_inverse(ugram / total_rows)
    u_next = jnp.dot(u_inverse, qt_piece, precision=HIGH)
    return (u_next, v_next, v_factor, u_factor)


def solution(mesh):
    n_row = mesh.shape["row"]
    n_col = mesh.shape["col"]
    lo = 1
    while lo * lo < n_row:
        lo *= 2
    grid = jax.sharding.Mesh(mesh.devices.reshape(n_row // lo, lo, n_col), ROW + ("col",))
    placed = (
        P(ROW, "col", None, None, None),
        P(ROW, "col", None),
        P(ROW, "col", None),
        P("col"),
        P(None, ROW),
        P(None, ("col",) + ROW),
        P(),
    )
    return jax.shard_map(
        per_device,
        mesh=grid,
        in_specs=placed,
        out_specs=(P(None, ROW + ("col",)), P(None, ("col",) + ROW), P(), P()),
        check_vma=False,
    )
```

```python
import math

import jax
import jax.numpy as jnp
from jax import lax
from jax.experimental import pallas as pl
from jax.sharding import PartitionSpec as P

HIGH = lax.Precision.HIGHEST
FAST = lax.Precision.HIGH


def _factor_kernel(aug_ref, low_ref, inv_ref):
    n = aug_ref.shape[0]
    whole = aug_ref[...]
    lane = lax.broadcasted_iota(jnp.int32, aug_ref.shape, 1)
    sub = lax.broadcasted_iota(jnp.int32, (n, 1), 0)
    low = jnp.zeros(aug_ref.shape, jnp.float32)
    for j in range(n):
        row = whole[j : j + 1, :]
        scale = lax.rsqrt(row[:, j : j + 1])
        scaled_row = row * scale
        inv_ref[j : j + 1, :] = scaled_row
        column = whole[:, j : j + 1] * scale
        whole = whole - jnp.where(sub > j, column, 0.0) * scaled_row
        low = jnp.where(lane == j, jnp.where(sub >= j, column, 0.0), low)
    low_ref[...] = low


def cholesky_and_inverse(gram):
    n = gram.shape[0]
    aug = jnp.concatenate([gram, jnp.eye(n, dtype=jnp.float32)], axis=1)
    low, inv = pl.pallas_call(
        _factor_kernel,
        out_shape=(
            jax.ShapeDtypeStruct(aug.shape, jnp.float32),
            jax.ShapeDtypeStruct(aug.shape, jnp.float32),
        ),
    )(aug)
    return low[:, :n], inv[:, n:]


ROW = ("row_hi", "row_lo")


def gather_sum(x, axis):
    n = lax.axis_size(axis)
    return lax.all_to_all(jnp.broadcast_to(x[None], (n,) + x.shape), axis, 0, 0, tiled=True).sum(0)


def per_device(tiles, tile_rows, tile_cols, exponents, u_basis, v_basis, prior):
    local_tiles = tiles[0, 0]
    rows_here = tile_rows[0, 0]
    cols_here = tile_cols[0, 0]
    count, tl, _ = local_tiles.shape
    width, block_rows = u_basis.shape
    block_cols = exponents.shape[0]
    rows_tiles = block_rows // tl
    cols_tiles = block_cols // tl
    n_row = lax.axis_size(ROW)
    n_col = lax.axis_size("col")
    total_rows = block_rows * n_row
    total_cols = block_cols * n_col
    v_piece = v_basis.shape[1]
    u_piece = block_rows // n_col
    col_scale = jnp.exp2(-exponents.astype(jnp.float32))
    lowtri = jnp.tril(prior)
    col_hits = (cols_here[:, None] == jnp.arange(cols_tiles, dtype=jnp.int32)[None, :]).astype(
        jnp.float32
    )
    row_hits = (rows_here[:, None] == jnp.arange(rows_tiles, dtype=jnp.int32)[None, :]).astype(
        jnp.float32
    )
    picked = jnp.take(u_basis.reshape(width, rows_tiles, tl), rows_here, axis=1)
    prod = jnp.einsum("sta,tab->stb", picked, local_tiles, precision=FAST)
    partial = jnp.einsum("stb,tc->csb", prod, col_hits, precision=FAST).reshape(
        n_row, v_piece // tl, width, tl
    )
    partial = (partial * col_scale.reshape(n_row, v_piece // tl, 1, tl)).transpose(0, 2, 1, 3)
    partial = partial.reshape(n_row, width, v_piece)
    received = lax.all_to_all(partial, ROW, 0, 0, tiled=True)
    pt_piece = received.sum(0) - jnp.dot(lowtri, v_basis, precision=HIGH)
    spread = jnp.broadcast_to(pt_piece[None], (n_row, width, v_piece))
    column = lax.all_to_all(spread, ROW, 0, 0, tiled=True)
    gram = gather_sum(jnp.einsum("jsb,jtb->st", column, column, precision=HIGH), "col")
    v_factor, v_inverse = cholesky_and_inverse(gram / total_cols)
    v_next = jnp.dot(v_inverse, pt_piece, precision=HIGH)
    factor = math.sqrt(total_rows / total_cols)
    scaled = column.transpose(1, 0, 2).reshape(width, block_cols) * col_scale
    chosen = jnp.take(scaled.reshape(width, cols_tiles, tl), cols_here, axis=1)
    products = jnp.einsum("stb,tab->sta", chosen, local_tiles, precision=FAST)
    terms = jnp.einsum("sta,tr->rsa", products, row_hits, precision=FAST)
    terms = terms.reshape(n_col, u_piece // tl, width, tl).transpose(0, 2, 1, 3)
    terms = terms.reshape(n_col, width, u_piece)
    summed = lax.all_to_all(terms, "col", 0, 0, tiled=True).sum(0)
    u_own = lax.dynamic_slice_in_dim(u_basis, lax.axis_index("col") * u_piece, u_piece, 1)
    qt_piece = factor * jnp.dot(v_inverse, summed, precision=HIGH) - jnp.dot(v_factor.T, u_own, precision=HIGH)
    ugram = jnp.dot(qt_piece, qt_piece.T, precision=HIGH)
    ugram = gather_sum(gather_sum(gather_sum(ugram, "col"), "row_lo"), "row_hi")
    u_factor, u_inverse = cholesky_and_inverse(ugram / total_rows)
    u_next = jnp.dot(u_inverse, qt_piece, precision=HIGH)
    return (u_next, v_next, v_factor, u_factor)


def solution(mesh):
    n_row = mesh.shape["row"]
    n_col = mesh.shape["col"]
    lo = 1
    while lo * lo < n_row:
        lo *= 2
    grid = jax.sharding.Mesh(mesh.devices.reshape(n_row // lo, lo, n_col), ROW + ("col",))
    placed = (
        P(ROW, "col", None, None, None),
        P(ROW, "col", None),
        P(ROW, "col", None),
        P("col"),
        P(None, ROW),
        P(None, ("col",) + ROW),
        P(),
    )
    return jax.shard_map(
        per_device,
        mesh=grid,
        in_specs=placed,
        out_specs=(P(None, ROW + ("col",)), P(None, ("col",) + ROW), P(), P()),
        check_vma=False,
    )
```

```python
import math

import jax
import jax.numpy as jnp
from jax import lax
from jax.experimental import pallas as pl
from jax.sharding import PartitionSpec as P

HIGH = lax.Precision.HIGHEST
FAST = lax.Precision.HIGH


def _factor_kernel(aug_ref, low_ref, inv_ref):
    n = aug_ref.shape[0]
    whole = aug_ref[...]
    lane = lax.broadcasted_iota(jnp.int32, aug_ref.shape, 1)
    sub = lax.broadcasted_iota(jnp.int32, (n, 1), 0)
    low = jnp.zeros(aug_ref.shape, jnp.float32)
    for j in range(n):
        row = whole[j : j + 1, :]
        scale = lax.rsqrt(row[:, j : j + 1])
        scaled_row = row * scale
        inv_ref[j : j + 1, :] = scaled_row
        column = whole[:, j : j + 1] * scale
        whole = whole - jnp.where(sub > j, column, 0.0) * scaled_row
        low = jnp.where(lane == j, jnp.where(sub >= j, column, 0.0), low)
    low_ref[...] = low


def cholesky_and_inverse(gram):
    n = gram.shape[0]
    aug = jnp.concatenate([gram, jnp.eye(n, dtype=jnp.float32)], axis=1)
    low, inv = pl.pallas_call(
        _factor_kernel,
        out_shape=(
            jax.ShapeDtypeStruct(aug.shape, jnp.float32),
            jax.ShapeDtypeStruct(aug.shape, jnp.float32),
        ),
    )(aug)
    return low[:, :n], inv[:, n:]


ROW = ("row_hi", "row_lo")


def gather_sum(x, axis):
    n = lax.axis_size(axis)
    return lax.all_to_all(jnp.broadcast_to(x[None], (n,) + x.shape), axis, 0, 0, tiled=True).sum(0)


def per_device(tiles, tile_rows, tile_cols, exponents, u_basis, v_basis, prior):
    local_tiles = tiles[0, 0]
    rows_here = tile_rows[0, 0]
    cols_here = tile_cols[0, 0]
    count, tl, _ = local_tiles.shape
    width, block_rows = u_basis.shape
    block_cols = exponents.shape[0]
    rows_tiles = block_rows // tl
    cols_tiles = block_cols // tl
    n_row = lax.axis_size(ROW)
    n_col = lax.axis_size("col")
    total_rows = block_rows * n_row
    total_cols = block_cols * n_col
    v_piece = v_basis.shape[1]
    u_piece = block_rows // n_col
    col_scale = jnp.exp2(-exponents.astype(jnp.float32))
    lowtri = jnp.tril(prior)
    row_hits = (rows_here[:, None] == jnp.arange(rows_tiles, dtype=jnp.int32)[None, :]).astype(
        jnp.float32
    )
    col_match = cols_here[:, None] == jnp.arange(cols_tiles, dtype=jnp.int32)[None, :]
    order = jnp.sum(jnp.where(col_match, jnp.arange(count, dtype=jnp.int32)[:, None], 0), axis=0)
    u_tiles = u_basis.reshape(width, rows_tiles, tl).transpose(1, 0, 2)
    picked = jnp.take(u_tiles, rows_here, axis=0)
    prod = jnp.einsum("tsa,tab->tsb", picked, local_tiles, precision=FAST)
    partial = jnp.take(prod, order, axis=0).reshape(n_row, v_piece // tl, width, tl)
    partial = (partial * col_scale.reshape(n_row, v_piece // tl, 1, tl)).transpose(0, 2, 1, 3)
    partial = partial.reshape(n_row, width, v_piece)
    received = lax.all_to_all(partial, ROW, 0, 0, tiled=True)
    pt_piece = received.sum(0) - jnp.dot(lowtri, v_basis, precision=HIGH)
    spread = jnp.broadcast_to(pt_piece[None], (n_row, width, v_piece))
    column = lax.all_to_all(spread, ROW, 0, 0, tiled=True)
    gram = gather_sum(jnp.einsum("jsb,jtb->st", column, column, precision=HIGH), "col")
    v_factor, v_inverse = cholesky_and_inverse(gram / total_cols)
    v_next = jnp.dot(v_inverse, pt_piece, precision=HIGH)
    factor = math.sqrt(total_rows / total_cols)
    scaled = column * col_scale.reshape(n_row, 1, v_piece)
    scaled = scaled.reshape(n_row, width, v_piece // tl, tl).transpose(0, 2, 1, 3)
    chosen = jnp.take(scaled.reshape(cols_tiles, width, tl), cols_here, axis=0)
    products = jnp.einsum("tsb,tab->tsa", chosen, local_tiles, precision=FAST)
    terms = jnp.einsum("tsa,tr->rsa", products, row_hits, precision=FAST)
    terms = terms.reshape(n_col, u_piece // tl, width, tl).transpose(0, 2, 1, 3)
    terms = terms.reshape(n_col, width, u_piece)
    summed = lax.all_to_all(terms, "col", 0, 0, tiled=True).sum(0)
    u_own = lax.dynamic_slice_in_dim(u_basis, lax.axis_index("col") * u_piece, u_piece, 1)
    qt_piece = factor * jnp.dot(v_inverse, summed, precision=HIGH) - jnp.dot(v_factor.T, u_own, precision=HIGH)
    ugram = jnp.dot(qt_piece, qt_piece.T, precision=HIGH)
    ugram = gather_sum(gather_sum(gather_sum(ugram, "col"), "row_lo"), "row_hi")
    u_factor, u_inverse = cholesky_and_inverse(ugram / total_rows)
    u_next = jnp.dot(u_inverse, qt_piece, precision=HIGH)
    return (u_next, v_next, v_factor, u_factor)


def solution(mesh):
    n_row = mesh.shape["row"]
    n_col = mesh.shape["col"]
    lo = 1
    while lo * lo < n_row:
        lo *= 2
    grid = jax.sharding.Mesh(mesh.devices.reshape(n_row // lo, lo, n_col), ROW + ("col",))
    placed = (
        P(ROW, "col", None, None, None),
        P(ROW, "col", None),
        P(ROW, "col", None),
        P("col"),
        P(None, ROW),
        P(None, ("col",) + ROW),
        P(),
    )
    return jax.shard_map(
        per_device,
        mesh=grid,
        in_specs=placed,
        out_specs=(P(None, ROW + ("col",)), P(None, ("col",) + ROW), P(), P()),
        check_vma=False,
    )
```

```python
import math

import jax
import jax.numpy as jnp
from jax import lax
from jax.experimental import pallas as pl
from jax.sharding import PartitionSpec as P

HIGH = lax.Precision.HIGHEST
FAST = lax.Precision.HIGH


def _factor_kernel(aug_ref, low_ref, inv_ref):
    n = aug_ref.shape[0]
    whole = aug_ref[...]
    lane = lax.broadcasted_iota(jnp.int32, low_ref.shape, 1)
    sub = lax.broadcasted_iota(jnp.int32, (n, 1), 0)
    low = jnp.zeros(low_ref.shape, jnp.float32)
    for j in range(n):
        row = whole[j : j + 1, :]
        scale = lax.rsqrt(row[:, j : j + 1])
        scaled_row = row * scale
        inv_ref[j : j + 1, :] = scaled_row
        column = whole[:, j : j + 1] * scale
        whole = whole - jnp.where(sub > j, column, 0.0) * scaled_row
        low = jnp.where(lane == j, jnp.where(sub >= j, column, 0.0), low)
    low_ref[...] = low


def cholesky_and_solve(gram, rhs):
    n = gram.shape[0]
    aug = jnp.concatenate([gram, rhs], axis=1)
    low, solved = pl.pallas_call(
        _factor_kernel,
        out_shape=(
            jax.ShapeDtypeStruct((n, max(n, 128)), jnp.float32),
            jax.ShapeDtypeStruct(aug.shape, jnp.float32),
        ),
    )(aug)
    return low[:, :n], solved[:, n:]


ROW = ("row_hi", "row_lo")


def gather_sum(x, axis):
    n = lax.axis_size(axis)
    return lax.all_to_all(jnp.broadcast_to(x[None], (n,) + x.shape), axis, 0, 0, tiled=True).sum(0)


def per_device(tiles, tile_rows, tile_cols, exponents, u_basis, v_basis, prior):
    local_tiles = tiles[0, 0]
    rows_here = tile_rows[0, 0]
    cols_here = tile_cols[0, 0]
    count, tl, _ = local_tiles.shape
    width, block_rows = u_basis.shape
    block_cols = exponents.shape[0]
    rows_tiles = block_rows // tl
    cols_tiles = block_cols // tl
    n_row = lax.axis_size(ROW)
    n_col = lax.axis_size("col")
    total_rows = block_rows * n_row
    total_cols = block_cols * n_col
    v_piece = v_basis.shape[1]
    u_piece = block_rows // n_col
    col_scale = jnp.exp2(-exponents.astype(jnp.float32))
    lowtri = jnp.tril(prior)
    row_hits = (rows_here[:, None] == jnp.arange(rows_tiles, dtype=jnp.int32)[None, :]).astype(
        jnp.float32
    )
    col_match = cols_here[:, None] == jnp.arange(cols_tiles, dtype=jnp.int32)[None, :]
    order = jnp.sum(jnp.where(col_match, jnp.arange(count, dtype=jnp.int32)[:, None], 0), axis=0)
    u_tiles = u_basis.reshape(width, rows_tiles, tl).transpose(1, 0, 2)
    picked = jnp.take(u_tiles, rows_here, axis=0)
    prod = jnp.einsum("tsa,tab->tsb", picked, local_tiles, precision=FAST)
    partial = jnp.take(prod, order, axis=0).reshape(n_row, v_piece // tl, width, tl)
    partial = (partial * col_scale.reshape(n_row, v_piece // tl, 1, tl)).transpose(0, 2, 1, 3)
    partial = partial.reshape(n_row, width, v_piece)
    received = lax.all_to_all(partial, ROW, 0, 0, tiled=True)
    pt_piece = received.sum(0) - jnp.dot(lowtri, v_basis, precision=HIGH)
    spread = jnp.broadcast_to(pt_piece[None], (n_row, width, v_piece))
    column = lax.all_to_all(spread, ROW, 0, 0, tiled=True)
    gram = gather_sum(jnp.einsum("jsb,jtb->st", column, column, precision=HIGH), "col")
    v_factor, v_inverse = cholesky_and_solve(gram / total_cols, jnp.eye(width, dtype=jnp.float32))
    v_next = jnp.dot(v_inverse, pt_piece, precision=HIGH)
    factor = math.sqrt(total_rows / total_cols)
    scaled = column * col_scale.reshape(n_row, 1, v_piece)
    scaled = scaled.reshape(n_row, width, v_piece // tl, tl).transpose(0, 2, 1, 3)
    chosen = jnp.take(scaled.reshape(cols_tiles, width, tl), cols_here, axis=0)
    products = jnp.einsum("tsb,tab->tsa", chosen, local_tiles, precision=FAST)
    terms = jnp.einsum("tsa,tr->rsa", products, row_hits, precision=FAST)
    terms = terms.reshape(n_col, u_piece // tl, width, tl).transpose(0, 2, 1, 3)
    terms = terms.reshape(n_col, width, u_piece)
    summed = lax.all_to_all(terms, "col", 0, 0, tiled=True).sum(0)
    u_own = lax.dynamic_slice_in_dim(u_basis, lax.axis_index("col") * u_piece, u_piece, 1)
    qt_piece = factor * jnp.dot(v_inverse, summed, precision=HIGH) - jnp.dot(v_factor.T, u_own, precision=HIGH)
    ugram = jnp.dot(qt_piece, qt_piece.T, precision=HIGH)
    ugram = gather_sum(gather_sum(gather_sum(ugram, "col"), "row_lo"), "row_hi")
    u_factor, u_next = cholesky_and_solve(ugram / total_rows, qt_piece)
    return (u_next, v_next, v_factor, u_factor)


def solution(mesh):
    n_row = mesh.shape["row"]
    n_col = mesh.shape["col"]
    lo = 1
    while lo * lo < n_row:
        lo *= 2
    grid = jax.sharding.Mesh(mesh.devices.reshape(n_row // lo, lo, n_col), ROW + ("col",))
    placed = (
        P(ROW, "col", None, None, None),
        P(ROW, "col", None),
        P(ROW, "col", None),
        P("col"),
        P(None, ROW),
        P(None, ("col",) + ROW),
        P(),
    )
    return jax.shard_map(
        per_device,
        mesh=grid,
        in_specs=placed,
        out_specs=(P(None, ROW + ("col",)), P(None, ("col",) + ROW), P(), P()),
        check_vma=False,
    )
```

```python
import math

import jax
import jax.numpy as jnp
from jax import lax
from jax.experimental import pallas as pl
from jax.sharding import PartitionSpec as P

HIGH = lax.Precision.HIGHEST
FAST = lax.Precision.HIGH


def _factor_kernel(aug_ref, low_ref, inv_ref):
    n = aug_ref.shape[0]
    whole = aug_ref[...]
    lane = lax.broadcasted_iota(jnp.int32, aug_ref.shape, 1)
    sub = lax.broadcasted_iota(jnp.int32, (n, 1), 0)
    low = jnp.zeros(aug_ref.shape, jnp.float32)
    for j in range(n):
        row = whole[j : j + 1, :]
        scale = lax.rsqrt(row[:, j : j + 1])
        scaled_row = row * scale
        inv_ref[j : j + 1, :] = scaled_row
        column = whole[:, j : j + 1] * scale
        whole = whole - jnp.where(sub > j, column, 0.0) * scaled_row
        low = jnp.where(lane == j, jnp.where(sub >= j, column, 0.0), low)
    low_ref[...] = low


def cholesky_and_inverse(gram):
    n = gram.shape[0]
    aug = jnp.concatenate([gram, jnp.eye(n, dtype=jnp.float32)], axis=1)
    low, inv = pl.pallas_call(
        _factor_kernel,
        out_shape=(
            jax.ShapeDtypeStruct(aug.shape, jnp.float32),
            jax.ShapeDtypeStruct(aug.shape, jnp.float32),
        ),
    )(aug)
    return low[:, :n], inv[:, n:]


ROW = ("row_hi", "row_lo")


def gather_sum(x, axis):
    n = lax.axis_size(axis)
    return lax.all_to_all(jnp.broadcast_to(x[None], (n,) + x.shape), axis, 0, 0, tiled=True).sum(0)


def per_device(tiles, tile_rows, tile_cols, exponents, u_basis, v_basis, prior):
    local_tiles = tiles[0, 0]
    rows_here = tile_rows[0, 0]
    cols_here = tile_cols[0, 0]
    count, tl, _ = local_tiles.shape
    width, block_rows = u_basis.shape
    block_cols = exponents.shape[0]
    rows_tiles = block_rows // tl
    cols_tiles = block_cols // tl
    n_row = lax.axis_size(ROW)
    n_col = lax.axis_size("col")
    total_rows = block_rows * n_row
    total_cols = block_cols * n_col
    v_piece = v_basis.shape[1]
    u_piece = block_rows // n_col
    col_scale = jnp.exp2(-exponents.astype(jnp.float32))
    lowtri = jnp.tril(prior)
    row_hits = (rows_here[:, None] == jnp.arange(rows_tiles, dtype=jnp.int32)[None, :]).astype(
        jnp.float32
    )
    col_match = cols_here[:, None] == jnp.arange(cols_tiles, dtype=jnp.int32)[None, :]
    order = jnp.sum(jnp.where(col_match, jnp.arange(count, dtype=jnp.int32)[:, None], 0), axis=0)
    u_tiles = u_basis.reshape(width, rows_tiles, tl).transpose(1, 0, 2)
    picked = jnp.take(u_tiles, rows_here, axis=0)
    prod = jnp.einsum("tsa,tab->tsb", picked, local_tiles, precision=FAST)
    partial = jnp.take(prod, order, axis=0).reshape(n_row, v_piece // tl, width, tl)
    partial = (partial * col_scale.reshape(n_row, v_piece // tl, 1, tl)).transpose(0, 2, 1, 3)
    partial = partial.reshape(n_row, width, v_piece)
    received = lax.all_to_all(partial, ROW, 0, 0, tiled=True)
    pt_piece = received.sum(0) - jnp.dot(lowtri, v_basis, precision=HIGH)
    spread = jnp.broadcast_to(pt_piece[None], (n_row, width, v_piece))
    column = lax.all_to_all(spread, ROW, 0, 0, tiled=True)
    gram = gather_sum(jnp.einsum("jsb,jtb->st", column, column, precision=HIGH), "col")
    v_factor, v_inverse = cholesky_and_inverse(gram / total_cols)
    v_next = jnp.dot(v_inverse, pt_piece, precision=HIGH)
    factor = math.sqrt(total_rows / total_cols)
    column_tiles = column.reshape(n_row, width, v_piece // tl, tl).transpose(0, 2, 1, 3)
    chosen = jnp.take(column_tiles.reshape(cols_tiles, width, tl), cols_here, axis=0)
    chosen = chosen * jnp.take(col_scale.reshape(cols_tiles, 1, tl), cols_here, axis=0)
    products = jnp.einsum("tsb,tab->tsa", chosen, local_tiles, precision=FAST)
    terms = jnp.einsum("tsa,tr->rsa", products, row_hits, precision=FAST)
    terms = terms.reshape(n_col, u_piece // tl, width, tl).transpose(0, 2, 1, 3)
    terms = terms.reshape(n_col, width, u_piece)
    summed = lax.all_to_all(terms, "col", 0, 0, tiled=True).sum(0)
    u_own = lax.dynamic_slice_in_dim(u_basis, lax.axis_index("col") * u_piece, u_piece, 1)
    qt_piece = factor * jnp.dot(v_inverse, summed, precision=HIGH) - jnp.dot(v_factor.T, u_own, precision=HIGH)
    ugram = jnp.dot(qt_piece, qt_piece.T, precision=HIGH)
    ugram = gather_sum(gather_sum(gather_sum(ugram, "col"), "row_lo"), "row_hi")
    u_factor, u_inverse = cholesky_and_inverse(ugram / total_rows)
    u_next = jnp.dot(u_inverse, qt_piece, precision=HIGH)
    return (u_next, v_next, v_factor, u_factor)


def solution(mesh):
    n_row = mesh.shape["row"]
    n_col = mesh.shape["col"]
    lo = 1
    while lo * lo < n_row:
        lo *= 2
    grid = jax.sharding.Mesh(mesh.devices.reshape(n_row // lo, lo, n_col), ROW + ("col",))
    placed = (
        P(ROW, "col", None, None, None),
        P(ROW, "col", None),
        P(ROW, "col", None),
        P("col"),
        P(None, ROW),
        P(None, ("col",) + ROW),
        P(),
    )
    return jax.shard_map(
        per_device,
        mesh=grid,
        in_specs=placed,
        out_specs=(P(None, ROW + ("col",)), P(None, ("col",) + ROW), P(), P()),
        check_vma=False,
    )
```

```python
import math

import jax
import jax.numpy as jnp
from jax import lax
from jax.experimental import pallas as pl
from jax.sharding import PartitionSpec as P

HIGH = lax.Precision.HIGHEST
FAST = lax.Precision.HIGH


def _factor_kernel(aug_ref, low_ref, inv_ref):
    n = aug_ref.shape[0]
    whole = aug_ref[...]
    lane = lax.broadcasted_iota(jnp.int32, aug_ref.shape, 1)
    sub = lax.broadcasted_iota(jnp.int32, (n, 1), 0)
    low = jnp.zeros(aug_ref.shape, jnp.float32)
    for j in range(n):
        row = whole[j : j + 1, :]
        scale = lax.rsqrt(row[:, j : j + 1])
        scaled_row = row * scale
        inv_ref[j : j + 1, :] = scaled_row
        column = whole[:, j : j + 1] * scale
        whole = whole - jnp.where(sub > j, column, 0.0) * scaled_row
        low = jnp.where(lane == j, jnp.where(sub >= j, column, 0.0), low)
    low_ref[...] = low


def cholesky_and_inverse(gram):
    n = gram.shape[0]
    aug = jnp.concatenate([gram, jnp.eye(n, dtype=jnp.float32)], axis=1)
    low, inv = pl.pallas_call(
        _factor_kernel,
        out_shape=(
            jax.ShapeDtypeStruct(aug.shape, jnp.float32),
            jax.ShapeDtypeStruct(aug.shape, jnp.float32),
        ),
    )(aug)
    return low[:, :n], inv[:, n:]


ROW = ("row_hi", "row_lo")


def gather_sum(x, axis):
    n = lax.axis_size(axis)
    return lax.all_to_all(jnp.broadcast_to(x[None], (n,) + x.shape), axis, 0, 0, tiled=True).sum(0)


def per_device(tiles, tile_rows, tile_cols, exponents, u_basis, v_basis, prior):
    local_tiles = tiles[0, 0]
    rows_here = tile_rows[0, 0]
    cols_here = tile_cols[0, 0]
    count, tl, _ = local_tiles.shape
    width, block_rows = u_basis.shape
    block_cols = exponents.shape[0]
    rows_tiles = block_rows // tl
    cols_tiles = block_cols // tl
    n_row = lax.axis_size(ROW)
    n_col = lax.axis_size("col")
    total_rows = block_rows * n_row
    total_cols = block_cols * n_col
    v_piece = v_basis.shape[1]
    u_piece = block_rows // n_col
    col_scale = jnp.exp2(-exponents.astype(jnp.float32))
    lowtri = jnp.tril(prior)
    tile_index = jnp.arange(count, dtype=jnp.int32)
    earlier = (rows_here[:, None] == rows_here[None, :]) & (tile_index[None, :] < tile_index[:, None])
    slot = rows_here * (count // rows_tiles) + jnp.sum(earlier.astype(jnp.int32), axis=1)
    row_order = jnp.sum(jnp.where(slot[:, None] == tile_index[None, :], tile_index[:, None], 0), axis=0)
    col_match = cols_here[:, None] == jnp.arange(cols_tiles, dtype=jnp.int32)[None, :]
    order = jnp.sum(jnp.where(col_match, jnp.arange(count, dtype=jnp.int32)[:, None], 0), axis=0)
    u_tiles = u_basis.reshape(width, rows_tiles, tl).transpose(1, 0, 2)
    picked = jnp.take(u_tiles, rows_here, axis=0)
    prod = jnp.einsum("tsa,tab->tsb", picked, local_tiles, precision=FAST)
    partial = jnp.take(prod, order, axis=0).reshape(n_row, v_piece // tl, width, tl)
    partial = (partial * col_scale.reshape(n_row, v_piece // tl, 1, tl)).transpose(0, 2, 1, 3)
    partial = partial.reshape(n_row, width, v_piece)
    received = lax.all_to_all(partial, ROW, 0, 0, tiled=True)
    pt_piece = received.sum(0) - jnp.dot(lowtri, v_basis, precision=HIGH)
    spread = jnp.broadcast_to(pt_piece[None], (n_row, width, v_piece))
    column = lax.all_to_all(spread, ROW, 0, 0, tiled=True)
    gram = gather_sum(jnp.einsum("jsb,jtb->st", column, column, precision=HIGH), "col")
    v_factor, v_inverse = cholesky_and_inverse(gram / total_cols)
    v_next = jnp.dot(v_inverse, pt_piece, precision=HIGH)
    factor = math.sqrt(total_rows / total_cols)
    column_tiles = column.reshape(n_row, width, v_piece // tl, tl).transpose(0, 2, 1, 3)
    chosen = jnp.take(column_tiles.reshape(cols_tiles, width, tl), cols_here, axis=0)
    chosen = chosen * jnp.take(col_scale.reshape(cols_tiles, 1, tl), cols_here, axis=0)
    products = jnp.einsum("tsb,tab->tsa", chosen, local_tiles, precision=FAST)
    reps = count // rows_tiles
    terms = jnp.take(products, row_order, axis=0).reshape(rows_tiles, reps, width, tl).sum(1)
    received_terms = lax.all_to_all(terms, "col", 0, 0, tiled=True)
    summed = received_terms.reshape(n_col, u_piece // tl, width, tl).sum(0)
    u_own = lax.dynamic_slice_in_dim(u_basis, lax.axis_index("col") * u_piece, u_piece, 1)
    qt_piece = factor * jnp.einsum("ij,rjb->irb", v_inverse, summed, precision=HIGH).reshape(width, u_piece) - jnp.dot(v_factor.T, u_own, precision=HIGH)
    ugram = jnp.dot(qt_piece, qt_piece.T, precision=HIGH)
    ugram = gather_sum(gather_sum(gather_sum(ugram, "col"), "row_lo"), "row_hi")
    u_factor, u_inverse = cholesky_and_inverse(ugram / total_rows)
    u_next = jnp.dot(u_inverse, qt_piece, precision=HIGH)
    return (u_next, v_next, v_factor, u_factor)


def solution(mesh):
    n_row = mesh.shape["row"]
    n_col = mesh.shape["col"]
    lo = 1
    while lo * lo < n_row:
        lo *= 2
    grid = jax.sharding.Mesh(mesh.devices.reshape(n_row // lo, lo, n_col), ROW + ("col",))
    placed = (
        P(ROW, "col", None, None, None),
        P(ROW, "col", None),
        P(ROW, "col", None),
        P("col"),
        P(None, ROW),
        P(None, ("col",) + ROW),
        P(),
    )
    return jax.shard_map(
        per_device,
        mesh=grid,
        in_specs=placed,
        out_specs=(P(None, ROW + ("col",)), P(None, ("col",) + ROW), P(), P()),
        check_vma=False,
    )
```

```python
import math

import jax
import jax.numpy as jnp
from jax import lax
from jax.experimental import pallas as pl
from jax.sharding import PartitionSpec as P

HIGH = lax.Precision.HIGHEST
FAST = lax.Precision.HIGH


def _factor_kernel(aug_ref, low_ref, inv_ref):
    n = aug_ref.shape[0]
    whole = aug_ref[...]
    lane = lax.broadcasted_iota(jnp.int32, aug_ref.shape, 1)
    sub = lax.broadcasted_iota(jnp.int32, (n, 1), 0)
    low = jnp.zeros(aug_ref.shape, jnp.float32)
    for j in range(n):
        row = whole[j : j + 1, :]
        scale = lax.rsqrt(row[:, j : j + 1])
        scaled_row = row * scale
        inv_ref[j : j + 1, :] = scaled_row
        column = whole[:, j : j + 1] * scale
        whole = whole - jnp.where(sub > j, column, 0.0) * scaled_row
        low = jnp.where(lane == j, jnp.where(sub >= j, column, 0.0), low)
    low_ref[...] = low


def cholesky_and_inverse(gram):
    n = gram.shape[0]
    aug = jnp.concatenate([gram, jnp.eye(n, dtype=jnp.float32)], axis=1)
    low, inv = pl.pallas_call(
        _factor_kernel,
        out_shape=(
            jax.ShapeDtypeStruct(aug.shape, jnp.float32),
            jax.ShapeDtypeStruct(aug.shape, jnp.float32),
        ),
    )(aug)
    return low[:, :n], inv[:, n:]


ROW = ("row_hi", "row_lo")


def gather_sum(x, axis):
    n = lax.axis_size(axis)
    return lax.all_to_all(jnp.broadcast_to(x[None], (n,) + x.shape), axis, 0, 0, tiled=True).sum(0)


def per_device(tiles, tile_rows, tile_cols, exponents, u_basis, v_basis, prior):
    local_tiles = tiles[0, 0]
    rows_here = tile_rows[0, 0]
    cols_here = tile_cols[0, 0]
    count, tl, _ = local_tiles.shape
    width, block_rows = u_basis.shape
    block_cols = exponents.shape[0]
    rows_tiles = block_rows // tl
    cols_tiles = block_cols // tl
    n_row = lax.axis_size(ROW)
    n_col = lax.axis_size("col")
    total_rows = block_rows * n_row
    total_cols = block_cols * n_col
    v_piece = v_basis.shape[1]
    u_piece = block_rows // n_col
    col_scale = jnp.exp2(-exponents.astype(jnp.float32))
    lowtri = jnp.tril(prior)
    row_hits = (rows_here[:, None] == jnp.arange(rows_tiles, dtype=jnp.int32)[None, :]).astype(
        jnp.float32
    )
    col_match = cols_here[:, None] == jnp.arange(cols_tiles, dtype=jnp.int32)[None, :]
    order = jnp.sum(jnp.where(col_match, jnp.arange(count, dtype=jnp.int32)[:, None], 0), axis=0)
    u_tiles = u_basis.reshape(width, rows_tiles, tl).transpose(1, 0, 2)
    picked = jnp.take(u_tiles, rows_here, axis=0)
    prod = jnp.einsum("tsa,tab->tsb", picked, local_tiles, precision=FAST)
    partial = jnp.take(prod, order, axis=0).reshape(n_row, v_piece // tl, width, tl)
    partial = (partial * col_scale.reshape(n_row, v_piece // tl, 1, tl)).transpose(0, 2, 1, 3)
    partial = partial.reshape(n_row, width, v_piece)
    received = lax.all_to_all(partial, ROW, 0, 0, tiled=True)
    pt_piece = received.sum(0) - jnp.dot(lowtri, v_basis, precision=HIGH)
    spread = jnp.broadcast_to(pt_piece[None], (n_row, width, v_piece))
    column = lax.all_to_all(spread, ROW, 0, 0, tiled=True)
    gram = gather_sum(jnp.einsum("jsb,jtb->st", column, column, precision=FAST), "col")
    v_factor, v_inverse = cholesky_and_inverse(gram / total_cols)
    v_next = jnp.dot(v_inverse, pt_piece, precision=HIGH)
    factor = math.sqrt(total_rows / total_cols)
    column_tiles = column.reshape(n_row, width, v_piece // tl, tl).transpose(0, 2, 1, 3)
    chosen = jnp.take(column_tiles.reshape(cols_tiles, width, tl), cols_here, axis=0)
    chosen = chosen * jnp.take(col_scale.reshape(cols_tiles, 1, tl), cols_here, axis=0)
    products = jnp.einsum("tsb,tab->tsa", chosen, local_tiles, precision=FAST)
    terms = jnp.einsum("tsa,tr->rsa", products, row_hits, precision=FAST)
    terms = terms.reshape(n_col, u_piece // tl, width, tl).transpose(0, 2, 1, 3)
    terms = terms.reshape(n_col, width, u_piece)
    summed = lax.all_to_all(terms, "col", 0, 0, tiled=True).sum(0)
    u_own = lax.dynamic_slice_in_dim(u_basis, lax.axis_index("col") * u_piece, u_piece, 1)
    qt_piece = factor * jnp.dot(v_inverse, summed, precision=HIGH) - jnp.dot(v_factor.T, u_own, precision=HIGH)
    ugram = jnp.dot(qt_piece, qt_piece.T, precision=HIGH)
    ugram = gather_sum(gather_sum(gather_sum(ugram, "col"), "row_lo"), "row_hi")
    u_factor, u_inverse = cholesky_and_inverse(ugram / total_rows)
    u_next = jnp.dot(u_inverse, qt_piece, precision=HIGH)
    return (u_next, v_next, v_factor, u_factor)


def solution(mesh):
    n_row = mesh.shape["row"]
    n_col = mesh.shape["col"]
    lo = 1
    while lo * lo < n_row:
        lo *= 2
    grid = jax.sharding.Mesh(mesh.devices.reshape(n_row // lo, lo, n_col), ROW + ("col",))
    placed = (
        P(ROW, "col", None, None, None),
        P(ROW, "col", None),
        P(ROW, "col", None),
        P("col"),
        P(None, ROW),
        P(None, ("col",) + ROW),
        P(),
    )
    return jax.shard_map(
        per_device,
        mesh=grid,
        in_specs=placed,
        out_specs=(P(None, ROW + ("col",)), P(None, ("col",) + ROW), P(), P()),
        check_vma=False,
    )
```

```python
import math

import jax
import jax.numpy as jnp
from jax import lax
from jax.experimental import pallas as pl
from jax.sharding import PartitionSpec as P

HIGH = lax.Precision.HIGHEST
FAST = lax.Precision.HIGH


def _factor_kernel(aug_ref, low_ref, inv_ref):
    n = aug_ref.shape[0]
    whole = aug_ref[...]
    lane = lax.broadcasted_iota(jnp.int32, aug_ref.shape, 1)
    sub = lax.broadcasted_iota(jnp.int32, (n, 1), 0)
    low = jnp.zeros(aug_ref.shape, jnp.float32)
    for j in range(n):
        row = whole[j : j + 1, :]
        scale = lax.rsqrt(row[:, j : j + 1])
        scaled_row = row * scale
        inv_ref[j : j + 1, :] = scaled_row
        column = whole[:, j : j + 1] * scale
        whole = whole - jnp.where(sub > j, column, 0.0) * scaled_row
        low = jnp.where(lane == j, jnp.where(sub >= j, column, 0.0), low)
    low_ref[...] = low


def cholesky_and_inverse(gram):
    n = gram.shape[0]
    aug = jnp.concatenate([gram, jnp.eye(n, dtype=jnp.float32)], axis=1)
    low, inv = pl.pallas_call(
        _factor_kernel,
        out_shape=(
            jax.ShapeDtypeStruct(aug.shape, jnp.float32),
            jax.ShapeDtypeStruct(aug.shape, jnp.float32),
        ),
    )(aug)
    return low[:, :n], inv[:, n:]


ROW = ("row_hi", "row_lo")


def gather_sum(x, axis):
    n = lax.axis_size(axis)
    return lax.all_to_all(jnp.broadcast_to(x[None], (n,) + x.shape), axis, 0, 0, tiled=True).sum(0)


def per_device(tiles, tile_rows, tile_cols, exponents, u_basis, v_basis, prior):
    local_tiles = tiles[0, 0]
    rows_here = tile_rows[0, 0]
    cols_here = tile_cols[0, 0]
    count, tl, _ = local_tiles.shape
    width, block_rows = u_basis.shape
    block_cols = exponents.shape[0]
    rows_tiles = block_rows // tl
    cols_tiles = block_cols // tl
    n_row = lax.axis_size(ROW)
    n_col = lax.axis_size("col")
    total_rows = block_rows * n_row
    total_cols = block_cols * n_col
    v_piece = v_basis.shape[1]
    u_piece = block_rows // n_col
    col_scale = jnp.exp2(-exponents.astype(jnp.float32))
    lowtri = jnp.tril(prior)
    row_hits = (rows_here[:, None] == jnp.arange(rows_tiles, dtype=jnp.int32)[None, :]).astype(
        jnp.float32
    )
    col_match = cols_here[:, None] == jnp.arange(cols_tiles, dtype=jnp.int32)[None, :]
    order = jnp.sum(jnp.where(col_match, jnp.arange(count, dtype=jnp.int32)[:, None], 0), axis=0)
    u_tiles = u_basis.reshape(width, rows_tiles, tl).transpose(1, 0, 2)
    picked = jnp.take(u_tiles, rows_here, axis=0)
    prod = jnp.einsum("tsa,tab->tsb", picked, local_tiles, precision=FAST)
    partial = jnp.take(prod, order, axis=0).reshape(n_row, v_piece // tl, width, tl)
    partial = (partial * col_scale.reshape(n_row, v_piece // tl, 1, tl)).transpose(0, 2, 1, 3)
    partial = partial.reshape(n_row, width, v_piece)
    received = lax.all_to_all(partial, ROW, 0, 0, tiled=True)
    pt_piece = received.sum(0) - jnp.dot(lowtri, v_basis, precision=HIGH)
    spread = jnp.broadcast_to(pt_piece[None], (n_row, width, v_piece))
    column = lax.all_to_all(spread, ROW, 0, 0, tiled=True)
    gram = gather_sum(jnp.einsum("jsb,jtb->st", column, column, precision=FAST), "col")
    v_factor, v_inverse = cholesky_and_inverse(gram / total_cols)
    v_next = jnp.dot(v_inverse, pt_piece, precision=HIGH)
    factor = math.sqrt(total_rows / total_cols)
    column_tiles = column.reshape(n_row, width, v_piece // tl, tl).transpose(0, 2, 1, 3)
    chosen = jnp.take(column_tiles.reshape(cols_tiles, width, tl), cols_here, axis=0)
    chosen = chosen * jnp.take(col_scale.reshape(cols_tiles, 1, tl), cols_here, axis=0)
    products = jnp.einsum("tsb,tab->tsa", chosen, local_tiles, precision=FAST)
    terms = jnp.einsum("tsa,tr->rsa", products, row_hits, precision=FAST)
    terms = terms.reshape(n_col, u_piece // tl, width, tl).transpose(0, 2, 1, 3)
    terms = terms.reshape(n_col, width, u_piece)
    summed = lax.all_to_all(terms, "col", 0, 0, tiled=True).sum(0)
    u_own = lax.dynamic_slice_in_dim(u_basis, lax.axis_index("col") * u_piece, u_piece, 1)
    qt_piece = factor * jnp.dot(v_inverse, summed, precision=FAST) - jnp.dot(v_factor.T, u_own, precision=FAST)
    ugram = jnp.dot(qt_piece, qt_piece.T, precision=FAST)
    ugram = gather_sum(gather_sum(gather_sum(ugram, "col"), "row_lo"), "row_hi")
    u_factor, u_inverse = cholesky_and_inverse(ugram / total_rows)
    u_next = jnp.dot(u_inverse, qt_piece, precision=HIGH)
    return (u_next, v_next, v_factor, u_factor)


def solution(mesh):
    n_row = mesh.shape["row"]
    n_col = mesh.shape["col"]
    lo = 1
    while lo * lo < n_row:
        lo *= 2
    grid = jax.sharding.Mesh(mesh.devices.reshape(n_row // lo, lo, n_col), ROW + ("col",))
    placed = (
        P(ROW, "col", None, None, None),
        P(ROW, "col", None),
        P(ROW, "col", None),
        P("col"),
        P(None, ROW),
        P(None, ("col",) + ROW),
        P(),
    )
    return jax.shard_map(
        per_device,
        mesh=grid,
        in_specs=placed,
        out_specs=(P(None, ROW + ("col",)), P(None, ("col",) + ROW), P(), P()),
        check_vma=False,
    )
```

```python
import math

import jax
import jax.numpy as jnp
from jax import lax
from jax.experimental import pallas as pl
from jax.sharding import PartitionSpec as P

HIGH = lax.Precision.HIGHEST
FAST = lax.Precision.HIGH


def _factor_kernel(aug_ref, low_ref, inv_ref):
    n = aug_ref.shape[0]
    whole = aug_ref[...]
    lane = lax.broadcasted_iota(jnp.int32, aug_ref.shape, 1)
    sub = lax.broadcasted_iota(jnp.int32, (n, 1), 0)
    low = jnp.zeros(aug_ref.shape, jnp.float32)
    for j in range(n):
        row = whole[j : j + 1, :]
        scale = lax.rsqrt(row[:, j : j + 1])
        scaled_row = row * scale
        inv_ref[j : j + 1, :] = scaled_row
        column = whole[:, j : j + 1] * scale
        whole = whole - jnp.where(sub > j, column, 0.0) * scaled_row
        low = jnp.where(lane == j, jnp.where(sub >= j, column, 0.0), low)
    low_ref[...] = low


def cholesky_and_inverse(gram):
    n = gram.shape[0]
    aug = jnp.concatenate([gram, jnp.eye(n, dtype=jnp.float32)], axis=1)
    low, inv = pl.pallas_call(
        _factor_kernel,
        out_shape=(
            jax.ShapeDtypeStruct(aug.shape, jnp.float32),
            jax.ShapeDtypeStruct(aug.shape, jnp.float32),
        ),
    )(aug)
    return low[:, :n], inv[:, n:]


ROW = ("row_hi", "row_lo")


def gather_sum(x, axis):
    n = lax.axis_size(axis)
    return lax.all_to_all(jnp.broadcast_to(x[None], (n,) + x.shape), axis, 0, 0, tiled=True).sum(0)


def per_device(tiles, tile_rows, tile_cols, exponents, u_basis, v_basis, prior):
    local_tiles = tiles[0, 0]
    rows_here = tile_rows[0, 0]
    cols_here = tile_cols[0, 0]
    count, tl, _ = local_tiles.shape
    width, block_rows = u_basis.shape
    block_cols = exponents.shape[0]
    rows_tiles = block_rows // tl
    cols_tiles = block_cols // tl
    n_row = lax.axis_size(ROW)
    n_col = lax.axis_size("col")
    total_rows = block_rows * n_row
    total_cols = block_cols * n_col
    v_piece = v_basis.shape[1]
    u_piece = block_rows // n_col
    col_scale = jnp.exp2(-exponents.astype(jnp.float32))
    lowtri = jnp.tril(prior)
    row_hits = (rows_here[:, None] == jnp.arange(rows_tiles, dtype=jnp.int32)[None, :]).astype(
        jnp.float32
    )
    col_match = cols_here[:, None] == jnp.arange(cols_tiles, dtype=jnp.int32)[None, :]
    order = jnp.sum(jnp.where(col_match, jnp.arange(count, dtype=jnp.int32)[:, None], 0), axis=0)
    u_tiles = u_basis.reshape(width, rows_tiles, tl).transpose(1, 0, 2)
    picked = jnp.take(u_tiles, rows_here, axis=0)
    prod = jnp.einsum("tsa,tab->tsb", picked, local_tiles, precision=FAST)
    partial = jnp.take(prod, order, axis=0).reshape(n_row, v_piece // tl, width, tl)
    partial = (partial * col_scale.reshape(n_row, v_piece // tl, 1, tl)).transpose(0, 2, 1, 3)
    partial = partial.reshape(n_row, width, v_piece)
    received = lax.all_to_all(partial, ROW, 0, 0, tiled=True)
    pt_piece = received.sum(0) - jnp.dot(lowtri, v_basis, precision=FAST)
    spread = jnp.broadcast_to(pt_piece[None], (n_row, width, v_piece))
    column = lax.all_to_all(spread, ROW, 0, 0, tiled=True)
    gram = gather_sum(jnp.einsum("jsb,jtb->st", column, column, precision=FAST), "col")
    v_factor, v_inverse = cholesky_and_inverse(gram / total_cols)
    v_next = jnp.dot(v_inverse, pt_piece, precision=HIGH)
    factor = math.sqrt(total_rows / total_cols)
    column_tiles = column.reshape(n_row, width, v_piece // tl, tl).transpose(0, 2, 1, 3)
    chosen = jnp.take(column_tiles.reshape(cols_tiles, width, tl), cols_here, axis=0)
    chosen = chosen * jnp.take(col_scale.reshape(cols_tiles, 1, tl), cols_here, axis=0)
    products = jnp.einsum("tsb,tab->tsa", chosen, local_tiles, precision=FAST)
    terms = jnp.einsum("tsa,tr->rsa", products, row_hits, precision=FAST)
    terms = terms.reshape(n_col, u_piece // tl, width, tl).transpose(0, 2, 1, 3)
    terms = terms.reshape(n_col, width, u_piece)
    summed = lax.all_to_all(terms, "col", 0, 0, tiled=True).sum(0)
    u_own = lax.dynamic_slice_in_dim(u_basis, lax.axis_index("col") * u_piece, u_piece, 1)
    qt_piece = factor * jnp.dot(v_inverse, summed, precision=HIGH) - jnp.dot(v_factor.T, u_own, precision=HIGH)
    ugram = jnp.dot(qt_piece, qt_piece.T, precision=HIGH)
    ugram = gather_sum(gather_sum(gather_sum(ugram, "col"), "row_lo"), "row_hi")
    u_factor, u_inverse = cholesky_and_inverse(ugram / total_rows)
    u_next = jnp.dot(u_inverse, qt_piece, precision=HIGH)
    return (u_next, v_next, v_factor, u_factor)


def solution(mesh):
    n_row = mesh.shape["row"]
    n_col = mesh.shape["col"]
    lo = 1
    while lo * lo < n_row:
        lo *= 2
    grid = jax.sharding.Mesh(mesh.devices.reshape(n_row // lo, lo, n_col), ROW + ("col",))
    placed = (
        P(ROW, "col", None, None, None),
        P(ROW, "col", None),
        P(ROW, "col", None),
        P("col"),
        P(None, ROW),
        P(None, ("col",) + ROW),
        P(),
    )
    return jax.shard_map(
        per_device,
        mesh=grid,
        in_specs=placed,
        out_specs=(P(None, ROW + ("col",)), P(None, ("col",) + ROW), P(), P()),
        check_vma=False,
    )
```
